128 devices in a mesh: blk: 16 (over y, x_hi, core), aux: 8 (over z, x_lo).
Axes of the slice: x: 4 (x_hi: 2, x_lo: 2; x = x_hi * 2 + x_lo), y: 4, z: 4, core: 2. Of those that a mesh axis runs over, the one named last changes fastest.
Arguments:
- three_center: bfloat16 [16, 16, 256, 128, 128], P('blk', None, 'aux'), may hold values from -6 to 6
- slab_factor: bfloat16 [256, 256, 256], P('aux'), may hold values from -0.0234375 to 0.0234375
- coefficients: bfloat16 [8192, 256], P('blk'), may hold values from -0.5 to 0.5
- tile_owner: int32 [16, 16, 1], P('blk'), may hold values from 0 to 15; in each aligned block of 16 rows (0 to 15, 16 to 31, ..., all dimensions but the last counted through in order) at most 2 rows name the same one
- tile_block: int32 [16, 16], P('blk'), may hold values from 0 to 3
- tile_lam: int32 [16, 16], P('blk'), may hold values from 0 to 3
Outputs:
- exchange_slab: float32 [64, 256, 128], P('blk', 'aux')
The draws below stay inside these ranges and needn't reach their ends.
Inputs may be any that keep to these rules, and one draw needn't show every extreme that they name: `tile_owner`: among the 16 tiles of one blk index at most 2 name the same owner, a bound that some block reaches.
All inputs are finite; a program needn't handle non-finite values.
Results may differ from the reference program's by a relative error of at most 0.0029.
Values may be sent and summed in bfloat16 or wider, within the bound.
No kernel may reach another device: no remote copies, remote signals or barrier semaphores. Data moves between devices by JAX's collectives and lax.ppermute only.
A program may use at most 128 MiB of HBM per device.

```python
import math
import jax
import jax.numpy as jnp
import numpy as np
from jax import lax

BS = 128
NOCC = 256
SLAB = 256
NB_DEV = 4
TPB = 1
CAP = 2
TILES_DEV = 16
NB = 64
NAUX = 256
N_BLK = 16


def place_ends(values, stream_key, low, largest):
    index_at = [jax.random.randint(jax.random.fold_in(stream_key, axis), (), 0, length) for axis, length in enumerate(values.shape)]
    longest = values.shape.index(max(values.shape))
    beside = index_at[:longest] + [(index_at[longest] + 1) % values.shape[longest]] + index_at[longest + 1:]
    return values.at[tuple(index_at)].set(low).at[tuple(beside)].set(largest)


def steps_of(key, dims, cuts, least, high):
    factor_of, own = 1.0, jax.random.fold_in(key, 6)
    for dim, shards_of in cuts:
        heights = jnp.exp(jax.random.uniform(jax.random.fold_in(own, dim), (shards_of,), jnp.float32, least / len(cuts), high / len(cuts)))
        factor_of = factor_of * jnp.repeat(heights, dims[dim] // shards_of).reshape([-1 if axis == dim else 1 for axis in range(len(dims))])
    return factor_of


def assign_block(own_key, own, number, rows, amount, top, bound, skew):
    sequence = jax.random.permutation(own_key, amount)
    packed, usual = shares(amount, rows * top, bound, skew, True), shares(amount, rows * top, bound, skew, False)
    places = jnp.arange(amount)

    def named(sizes, offset_by):
        used = int((sizes > 0).sum())
        fixed = max(1, used // 4)
        moved = fixed + (places - fixed + offset_by * (used - fixed)) % max(1, amount - fixed)
        return jnp.zeros((amount,), jnp.int32).at[sequence[jnp.where(places < fixed, places, moved)]].set(jnp.asarray(sizes, jnp.int32))

    sizes = jnp.where(number % 4 == 0, named(packed, number // 4), named(usual, number - number // 4 - 1))
    mixed = jax.random.permutation(jax.random.fold_in(own, 3), amount)
    source_of, taker = mixed[0:amount // 2 * 2:2], mixed[1:amount // 2 * 2:2]
    room = jnp.minimum(sizes[source_of] - 1, bound - sizes[taker]) // 2
    room = jnp.where((source_of == sequence[0]) | (taker == sequence[0]) | (sizes[taker] == 0), 0, jnp.maximum(room, 0))
    moved = jax.random.randint(jax.random.fold_in(own, 4), (amount // 2,), 0, 1 << 20) % (room + 1)
    sizes = sizes.at[source_of].add(-moved).at[taker].add(moved)
    members = jnp.searchsorted(jnp.cumsum(sizes), jnp.arange(rows * top), side="right").astype(jnp.int32)
    listing = members.reshape(top, rows).T
    listing = listing[jax.random.permutation(jax.random.fold_in(own, 1), rows)]
    offset_by = jax.random.randint(jax.random.fold_in(own, 2), (rows, 1), 0, top)
    return jnp.take_along_axis(listing, (jnp.arange(top)[None, :] + offset_by) % top, axis=1)


def shares(amount, total, reach, skew, full):
    portions = [(1 << 20) // math.isqrt(standing ** skew) + 1 for standing in range(1, amount + 1)]
    largest = reach if full else min(reach, max(-(-total // amount), total * portions[0] // sum(portions)))
    least = 1 if total - largest >= amount - 1 else 0
    counts, surplus = [largest] + [least] * (amount - 1), total - largest - least * (amount - 1)
    while surplus > 0:
        candidates = [i for i in range(1, amount) if counts[i] < largest] or [i for i in range(1, amount) if counts[i] < reach]
        whole, remaining = sum([portions[i] for i in candidates]), surplus
        for i in candidates:
            extra = min(reach - counts[i], max(1, remaining * portions[i] // whole), surplus)
            counts[i] = counts[i] + extra
            surplus = surplus - extra
    return np.array(counts)


def noise(stream_key, dims, scale, bound, split=(), held_as=jnp.bfloat16):
    array = jax.random.normal(stream_key, dims, jnp.float32) * scale
    if len(split) > 0:
        array = steps_of(stream_key, dims, split, -0.22, 0.18) * array
    return jnp.clip(array, min=-bound, max=bound).astype(held_as)


def setup_inputs(seed: int = 0) -> dict:
    key_list = jax.random.split(jax.random.key(seed), 7)
    three_center = noise(key_list[0], (N_BLK, TILES_DEV, NAUX, BS, BS), 1.0, 6.0, ((0, 16), (2, 8)))
    slab_factor = noise(key_list[1], (NAUX, SLAB, NOCC), (NAUX * NOCC) ** -0.5, 0.0234375, ((0, 8),))
    coefficients = noise(key_list[2], (NB * BS, NOCC), BS ** -0.5, 0.5, ((0, 16),))
    tile_owner_keys = jax.random.split(jax.random.fold_in(key_list[3], 1), N_BLK * TILES_DEV // TILES_DEV)
    tile_owner_turns = jax.random.permutation(jax.random.fold_in(key_list[3], 3), N_BLK * TILES_DEV // TILES_DEV)
    tile_owner = jax.vmap(lambda own, number: assign_block(jax.random.fold_in(key_list[3], 2), own, number, TILES_DEV, N_BLK, 1, CAP, 2))(tile_owner_keys, tile_owner_turns).reshape((N_BLK, TILES_DEV, 1))
    tile_block = place_ends(jax.random.randint(key_list[4], (N_BLK, TILES_DEV), 0, NB_DEV), jax.random.fold_in(key_list[4], 1), 0, NB_DEV - 1).astype(jnp.int32)
    tile_lam = place_ends(jax.random.randint(key_list[5], (N_BLK, TILES_DEV), 0, NB_DEV), jax.random.fold_in(key_list[5], 1), 0, NB_DEV - 1).astype(jnp.int32)
    return {"three_center": three_center, "slab_factor": slab_factor, "coefficients": coefficients, "tile_owner": tile_owner, "tile_block": tile_block, "tile_lam": tile_lam}


def reference(three_center, slab_factor, coefficients, tile_owner, tile_block, tile_lam):
    total_tiles = N_BLK * TILES_DEV
    flat_data = three_center.reshape(total_tiles, NAUX, BS, BS)
    tile_ids = jnp.arange(total_tiles, dtype=jnp.int32)
    group_of = (tile_ids % TILES_DEV) // TPB
    lam_block = (group_of * NB_DEV + tile_lam.reshape(-1)).astype(jnp.int32)
    target = (tile_owner.reshape(-1) * NB_DEV + tile_block.reshape(-1)).astype(jnp.int32)
    slab_wide = slab_factor.astype(jnp.float32)
    panels = coefficients.reshape(NB, BS, NOCC)

    def add_tile(running, items):
        tile_data, lam_index, slot_index = items
        panel = lax.dynamic_index_in_dim(panels, lam_index, 0, keepdims=False)
        half_tile = jnp.einsum("pxl,li->pxi", tile_data.astype(jnp.float32), panel.astype(jnp.float32)).astype(jnp.bfloat16)
        partial_value = jnp.einsum("pmi,pxi->mx", slab_wide, half_tile.astype(jnp.float32))
        return running.at[slot_index].add(partial_value), None

    initial = jnp.zeros((NB, SLAB, BS), jnp.float32)
    result, _ = lax.scan(add_tile, initial, (flat_data, lam_block, target))
    return result
```

```python
import functools

import jax
import jax.numpy as jnp
from jax import lax
from jax.experimental import pallas as pl
from jax.experimental.pallas import tpu as pltpu
from jax.sharding import PartitionSpec as P

CAP = 2
P_CHUNK = 8


def tile_kernel(t_ref, c_ref, s_ref, o_ref):
    n_p, bs, _ = t_ref.shape
    panel = c_ref[...]
    acc = None
    for c0 in range(0, n_p, P_CHUNK):
        block = t_ref[c0:c0 + P_CHUNK].reshape(P_CHUNK * bs, bs)
        half = jnp.dot(block, panel, preferred_element_type=jnp.float32).astype(jnp.bfloat16)
        for j in range(P_CHUNK):
            term = lax.dot_general(
                s_ref[c0 + j],
                half[j * bs:(j + 1) * bs],
                (((1,), (1,)), ((), ())),
                preferred_element_type=jnp.float32,
            )
            acc = term if acc is None else acc + term
    o_ref[...] = acc.reshape(o_ref.shape)


def tile_partials(tile_data, panels, slab_factor, n_aux):
    tiles, n_p, bs, _ = tile_data.shape
    occ = panels.shape[2]
    slab = slab_factor.shape[1]
    rows = slab // n_aux
    flops = tiles * (2 * n_p * bs * bs * occ + 2 * n_p * slab * occ * bs)
    bytes_accessed = tile_data.size * 2 + panels.size * 2 + slab_factor.size * 2 + tiles * slab * bs * 4
    return pl.pallas_call(
        tile_kernel,
        grid=(tiles,),
        in_specs=[
            pl.BlockSpec((None, n_p, bs, bs), lambda t: (t, 0, 0, 0)),
            pl.BlockSpec((None, bs, occ), lambda t: (t, 0, 0)),
            pl.BlockSpec((n_p, slab, occ), lambda t: (0, 0, 0)),
        ],
        out_specs=pl.BlockSpec((n_aux, None, rows, bs), lambda t: (0, t, 0, 0)),
        out_shape=jax.ShapeDtypeStruct((n_aux, tiles, rows, bs), jnp.float32),
        cost_estimate=pl.CostEstimate(flops=flops, transcendentals=0, bytes_accessed=bytes_accessed),
    )(tile_data, panels, slab_factor)


def local(three_center, slab_factor, coefficients, tile_owner, tile_block, tile_lam):
    tile_data = three_center[0]
    n_blk = lax.axis_size("blk")
    n_aux = lax.axis_size("aux")
    tiles = tile_data.shape[0]
    per_group = tiles // n_blk
    bs = tile_data.shape[2]
    rows_dev, occ = coefficients.shape
    blocks_dev = rows_dev // bs

    owner_ids = tile_owner[0, :, 0]
    block_ids = tile_block[0]
    lam_ids = tile_lam[0]

    same_owner = owner_ids[:, None] == owner_ids[None, :]
    earlier = jnp.arange(tiles)[None, :] < jnp.arange(tiles)[:, None]
    slot_rank = jnp.sum((same_owner & earlier).astype(jnp.int32), axis=1)
    position = owner_ids * CAP + slot_rank
    slot_hit = jnp.arange(n_blk * CAP, dtype=jnp.int32)[:, None] == position[None, :]
    slot_valid = jnp.any(slot_hit, axis=1)
    slot_tile = jnp.sum(jnp.where(slot_hit, jnp.arange(tiles, dtype=jnp.int32)[None, :], 0), axis=1)
    slot_label = jnp.where(slot_valid, block_ids[slot_tile], -1)

    ints = jnp.concatenate(
        [lam_ids.reshape(n_blk, per_group), slot_label.reshape(n_blk, CAP)], axis=1
    ).astype(jnp.int32)
    ints_got = lax.all_to_all(ints, "blk", 0, 0, tiled=True)
    lam_req = ints_got[:, :per_group]
    got_labels = ints_got[:, per_group:]

    coef_blocks = coefficients.reshape(blocks_dev, bs, occ)
    send_panels = coef_blocks[lam_req.reshape(-1)].reshape(n_blk, per_group, bs, occ)
    panels = lax.all_to_all(send_panels, "blk", 0, 0, tiled=True).reshape(tiles, bs, occ)

    partial = tile_partials(tile_data, panels, slab_factor, n_aux)
    reduced = lax.psum_scatter(partial, "aux", scatter_dimension=0, tiled=True)[0]

    picked = reduced[slot_tile]
    send_tiles = jnp.where(slot_valid[:, None, None], picked, 0.0)
    send_tiles = send_tiles.reshape((n_blk, CAP) + send_tiles.shape[1:])
    received = lax.all_to_all(send_tiles, "blk", 0, 0, tiled=True)
    received = received.reshape((n_blk * CAP,) + received.shape[2:])
    labels = got_labels.reshape(-1)
    owned = jnp.stack(
        [jnp.sum(jnp.where((labels == b)[:, None, None], received, 0.0), axis=0) for b in range(blocks_dev)]
    )
    return owned


def solution(mesh):
    placed = (
        P("blk", None, "aux", None, None),
        P("aux", None, None),
        P("blk", None),
        P("blk", None, None),
        P("blk", None),
        P("blk", None),
    )
    return jax.shard_map(
        local, mesh=mesh, in_specs=placed, out_specs=P("blk", "aux", None), check_vma=False
    )
```

```python
import functools

import jax
import jax.numpy as jnp
from jax import lax
from jax.experimental import pallas as pl
from jax.experimental.pallas import tpu as pltpu
from jax.sharding import PartitionSpec as P

CAP = 2
P_CHUNK = 4
ROW_CHUNK = 512


def tile_kernel(t_ref, c_ref, s_ref, o_ref, hbuf, acc):
    step = pl.program_id(0)
    tiles, n_p, bs, _ = t_ref.shape
    occ = c_ref.shape[2]

    @pl.when(step == 0)
    def _():
        acc[...] = jnp.zeros_like(acc)

    for t in range(tiles):
        block = t_ref[t].reshape(n_p * bs, bs)
        half = jnp.dot(block, c_ref[t], preferred_element_type=jnp.float32).astype(jnp.bfloat16)
        for j in range(n_p):
            hbuf[t * bs:(t + 1) * bs, j * occ:(j + 1) * occ] = half[j * bs:(j + 1) * bs]
    for r in range(0, tiles * bs, ROW_CHUNK):
        acc[r:r + ROW_CHUNK] += jnp.dot(
            hbuf[r:r + ROW_CHUNK], s_ref[...], preferred_element_type=jnp.float32
        )

    @pl.when(step == pl.num_programs(0) - 1)
    def _():
        for t in range(tiles):
            o_ref[:, t] = acc[t * bs:(t + 1) * bs].T.reshape(o_ref.shape[0], o_ref.shape[2], o_ref.shape[3])


def tile_partials(tile_data, panels, slab_t, n_aux):
    tiles, n_p, bs, _ = tile_data.shape
    occ = panels.shape[2]
    slab = slab_t.shape[1]
    rows = slab // n_aux
    flops = tiles * (2 * n_p * bs * bs * occ + 2 * n_p * slab * occ * bs)
    bytes_accessed = tile_data.size * 2 + panels.size * 2 + slab_t.size * 2 + tiles * slab * bs * 4
    return pl.pallas_call(
        tile_kernel,
        grid=(n_p // P_CHUNK,),
        in_specs=[
            pl.BlockSpec((tiles, P_CHUNK, bs, bs), lambda c: (0, c, 0, 0)),
            pl.BlockSpec((tiles, bs, occ), lambda c: (0, 0, 0)),
            pl.BlockSpec((P_CHUNK * occ, slab), lambda c: (c, 0)),
        ],
        out_specs=pl.BlockSpec((n_aux, tiles, rows, bs), lambda c: (0, 0, 0, 0)),
        out_shape=jax.ShapeDtypeStruct((n_aux, tiles, rows, bs), jnp.float32),
        scratch_shapes=[
            pltpu.VMEM((tiles * bs, P_CHUNK * occ), jnp.bfloat16),
            pltpu.VMEM((tiles * bs, slab), jnp.float32),
        ],
        compiler_params=pltpu.CompilerParams(vmem_limit_bytes=48 * 1024 * 1024),
        cost_estimate=pl.CostEstimate(flops=flops, transcendentals=0, bytes_accessed=bytes_accessed),
    )(tile_data, panels, slab_t)


def local(three_center, slab_factor, coefficients, tile_owner, tile_block, tile_lam):
    tile_data = three_center[0]
    n_blk = lax.axis_size("blk")
    n_aux = lax.axis_size("aux")
    tiles = tile_data.shape[0]
    per_group = tiles // n_blk
    bs = tile_data.shape[2]
    rows_dev, occ = coefficients.shape
    blocks_dev = rows_dev // bs

    owner_ids = tile_owner[0, :, 0]
    block_ids = tile_block[0]
    lam_ids = tile_lam[0]

    same_owner = owner_ids[:, None] == owner_ids[None, :]
    earlier = jnp.arange(tiles)[None, :] < jnp.arange(tiles)[:, None]
    slot_rank = jnp.sum((same_owner & earlier).astype(jnp.int32), axis=1)
    position = owner_ids * CAP + slot_rank
    slot_hit = jnp.arange(n_blk * CAP, dtype=jnp.int32)[:, None] == position[None, :]
    slot_valid = jnp.any(slot_hit, axis=1)
    slot_tile = jnp.sum(jnp.where(slot_hit, jnp.arange(tiles, dtype=jnp.int32)[None, :], 0), axis=1)
    slot_label = jnp.where(slot_valid, block_ids[slot_tile], -1)

    ints = jnp.concatenate(
        [lam_ids.reshape(n_blk, per_group), slot_label.reshape(n_blk, CAP)], axis=1
    ).astype(jnp.int32)
    ints_got = lax.all_to_all(ints, "blk", 0, 0, tiled=True)
    lam_req = ints_got[:, :per_group]
    got_labels = ints_got[:, per_group:]

    coef_blocks = coefficients.reshape(blocks_dev, bs, occ)
    send_panels = coef_blocks[lam_req.reshape(-1)].reshape(n_blk, per_group, bs, occ)
    panels = lax.all_to_all(send_panels, "blk", 0, 0, tiled=True).reshape(tiles, bs, occ)

    n_p, slab = slab_factor.shape[0], slab_factor.shape[1]
    slab_t = jnp.swapaxes(slab_factor, 1, 2).reshape(n_p * occ, slab)
    partial = tile_partials(tile_data, panels, slab_t, n_aux)
    reduced = jnp.sum(lax.all_to_all(partial, "aux", 0, 0, tiled=True), axis=0)

    picked = reduced[slot_tile]
    send_tiles = jnp.where(slot_valid[:, None, None], picked, 0.0)
    send_tiles = send_tiles.reshape((n_blk, CAP) + send_tiles.shape[1:])
    received = lax.all_to_all(send_tiles, "blk", 0, 0, tiled=True)
    received = received.reshape((n_blk * CAP,) + received.shape[2:])
    labels = got_labels.reshape(-1)
    owned = jnp.stack(
        [jnp.sum(jnp.where((labels == b)[:, None, None], received, 0.0), axis=0) for b in range(blocks_dev)]
    )
    return owned


def solution(mesh):
    placed = (
        P("blk", None, "aux", None, None),
        P("aux", None, None),
        P("blk", None),
        P("blk", None, None),
        P("blk", None),
        P("blk", None),
    )
    return jax.shard_map(
        local, mesh=mesh, in_specs=placed, out_specs=P("blk", "aux", None), check_vma=False
    )
```

```python
import functools

import jax
import jax.numpy as jnp
from jax import lax
from jax.experimental import pallas as pl
from jax.experimental.pallas import tpu as pltpu
from jax.sharding import PartitionSpec as P

CAP = 2
P_CHUNK = 8
ROW_CHUNK = 512


def tile_kernel(t_ref, c_ref, s_ref, o_ref, hbuf, acc):
    step = pl.program_id(0)
    tiles, n_p, bs, _ = t_ref.shape
    occ = c_ref.shape[2]

    @pl.when(step == 0)
    def _():
        acc[...] = jnp.zeros_like(acc)

    for t in range(tiles):
        block = t_ref[t].reshape(n_p * bs, bs)
        half = jnp.dot(block, c_ref[t], preferred_element_type=jnp.float32).astype(jnp.bfloat16)
        for j in range(n_p):
            hbuf[t * bs:(t + 1) * bs, j * occ:(j + 1) * occ] = half[j * bs:(j + 1) * bs]
    for r in range(0, tiles * bs, ROW_CHUNK):
        acc[r:r + ROW_CHUNK] += jnp.dot(
            hbuf[r:r + ROW_CHUNK], s_ref[...], preferred_element_type=jnp.float32
        )

    @pl.when(step == pl.num_programs(0) - 1)
    def _():
        for t in range(tiles):
            o_ref[:, t] = acc[t * bs:(t + 1) * bs].T.reshape(o_ref.shape[0], o_ref.shape[2], o_ref.shape[3])


def tile_partials(tile_data, panels, slab_t, n_aux):
    tiles, n_p, bs, _ = tile_data.shape
    occ = panels.shape[2]
    slab = slab_t.shape[1]
    rows = slab // n_aux
    flops = tiles * (2 * n_p * bs * bs * occ + 2 * n_p * slab * occ * bs)
    bytes_accessed = tile_data.size * 2 + panels.size * 2 + slab_t.size * 2 + tiles * slab * bs * 4
    return pl.pallas_call(
        tile_kernel,
        grid=(n_p // P_CHUNK,),
        in_specs=[
            pl.BlockSpec((tiles, P_CHUNK, bs, bs), lambda c: (0, c, 0, 0)),
            pl.BlockSpec((tiles, bs, occ), lambda c: (0, 0, 0)),
            pl.BlockSpec((P_CHUNK * occ, slab), lambda c: (c, 0)),
        ],
        out_specs=pl.BlockSpec((n_aux, tiles, rows, bs), lambda c: (0, 0, 0, 0)),
        out_shape=jax.ShapeDtypeStruct((n_aux, tiles, rows, bs), jnp.float32),
        scratch_shapes=[
            pltpu.VMEM((tiles * bs, P_CHUNK * occ), jnp.bfloat16),
            pltpu.VMEM((tiles * bs, slab), jnp.float32),
        ],
        compiler_params=pltpu.CompilerParams(vmem_limit_bytes=48 * 1024 * 1024),
        cost_estimate=pl.CostEstimate(flops=flops, transcendentals=0, bytes_accessed=bytes_accessed),
    )(tile_data, panels, slab_t)


def local(three_center, slab_factor, coefficients, tile_owner, tile_block, tile_lam):
    tile_data = three_center[0]
    n_blk = lax.axis_size("blk")
    n_aux = lax.axis_size("aux")
    tiles = tile_data.shape[0]
    per_group = tiles // n_blk
    bs = tile_data.shape[2]
    rows_dev, occ = coefficients.shape
    blocks_dev = rows_dev // bs

    owner_ids = tile_owner[0, :, 0]
    block_ids = tile_block[0]
    lam_ids = tile_lam[0]

    same_owner = owner_ids[:, None] == owner_ids[None, :]
    earlier = jnp.arange(tiles)[None, :] < jnp.arange(tiles)[:, None]
    slot_rank = jnp.sum((same_owner & earlier).astype(jnp.int32), axis=1)
    position = owner_ids * CAP + slot_rank
    slot_hit = jnp.arange(n_blk * CAP, dtype=jnp.int32)[:, None] == position[None, :]
    slot_valid = jnp.any(slot_hit, axis=1)
    slot_tile = jnp.sum(jnp.where(slot_hit, jnp.arange(tiles, dtype=jnp.int32)[None, :], 0), axis=1)
    slot_label = jnp.where(slot_valid, block_ids[slot_tile], -1)

    lam_req = lax.all_to_all(lam_ids.reshape(n_blk, per_group), "blk", 0, 0, tiled=True)

    coef_blocks = coefficients.reshape(blocks_dev, bs, occ)
    send_panels = coef_blocks[lam_req.reshape(-1)].reshape(n_blk, per_group, bs, occ)
    panels = lax.all_to_all(send_panels, "blk", 0, 0, tiled=True).reshape(tiles, bs, occ)

    n_p, slab = slab_factor.shape[0], slab_factor.shape[1]
    slab_t = jnp.swapaxes(slab_factor, 1, 2).reshape(n_p * occ, slab)
    partial = tile_partials(tile_data, panels, slab_t, n_aux)
    reduced = jnp.sum(lax.all_to_all(partial, "aux", 0, 0, tiled=True), axis=0)

    picked = reduced[slot_tile]
    send_tiles = jnp.where(slot_valid[:, None, None], picked, 0.0)
    label_rows = jnp.broadcast_to(slot_label.astype(jnp.float32)[:, None, None], (n_blk * CAP, 8, bs))
    rows = send_tiles.shape[1]
    send_tiles = jnp.concatenate([send_tiles, label_rows], axis=1)
    send_tiles = send_tiles.reshape((n_blk, CAP) + send_tiles.shape[1:])
    received = lax.all_to_all(send_tiles, "blk", 0, 0, tiled=True)
    received = received.reshape((n_blk * CAP,) + received.shape[2:])
    labels = received[:, rows, 0]
    data = received[:, :rows]
    owned = jnp.stack(
        [jnp.sum(jnp.where((labels == b)[:, None, None], data, 0.0), axis=0) for b in range(blocks_dev)]
    )
    return owned


def solution(mesh):
    placed = (
        P("blk", None, "aux", None, None),
        P("aux", None, None),
        P("blk", None),
        P("blk", None, None),
        P("blk", None),
        P("blk", None),
    )
    return jax.shard_map(
        local, mesh=mesh, in_specs=placed, out_specs=P("blk", "aux", None), check_vma=False
    )
```

```python
import functools

import jax
import jax.numpy as jnp
from jax import lax
from jax.experimental import pallas as pl
from jax.experimental.pallas import tpu as pltpu
from jax.sharding import PartitionSpec as P

CAP = 2
P_CHUNK = 4
ROW_CHUNK = 512


def tile_kernel(t_ref, c_ref, s_ref, o_ref, hbuf, acc):
    step = pl.program_id(0)
    tiles, n_p, bs, _ = t_ref.shape
    occ = c_ref.shape[2]

    @pl.when(step == 0)
    def _():
        acc[...] = jnp.zeros_like(acc)

    for t in range(tiles):
        block = t_ref[t].reshape(n_p * bs, bs)
        half = jnp.dot(block, c_ref[t], preferred_element_type=jnp.float32).astype(jnp.bfloat16)
        for j in range(n_p):
            hbuf[t * bs:(t + 1) * bs, j * occ:(j + 1) * occ] = half[j * bs:(j + 1) * bs]
    for r in range(0, tiles * bs, ROW_CHUNK):
        acc[r:r + ROW_CHUNK] += jnp.dot(
            hbuf[r:r + ROW_CHUNK], s_ref[...], preferred_element_type=jnp.float32
        )

    @pl.when(step == pl.num_programs(0) - 1)
    def _():
        for t in range(tiles):
            o_ref[:, t] = acc[t * bs:(t + 1) * bs].T.reshape(o_ref.shape[0], o_ref.shape[2], o_ref.shape[3])


def tile_partials(tile_data, panels, slab_t, n_aux):
    tiles, n_p, bs, _ = tile_data.shape
    occ = panels.shape[2]
    slab = slab_t.shape[1]
    rows = slab // n_aux
    flops = tiles * (2 * n_p * bs * bs * occ + 2 * n_p * slab * occ * bs)
    bytes_accessed = tile_data.size * 2 + panels.size * 2 + slab_t.size * 2 + tiles * slab * bs * 4
    return pl.pallas_call(
        tile_kernel,
        grid=(n_p // P_CHUNK,),
        in_specs=[
            pl.BlockSpec((tiles, P_CHUNK, bs, bs), lambda c: (0, c, 0, 0)),
            pl.BlockSpec((tiles, bs, occ), lambda c: (0, 0, 0)),
            pl.BlockSpec((P_CHUNK * occ, slab), lambda c: (c, 0)),
        ],
        out_specs=pl.BlockSpec((n_aux, tiles, rows, bs), lambda c: (0, 0, 0, 0)),
        out_shape=jax.ShapeDtypeStruct((n_aux, tiles, rows, bs), jnp.float32),
        scratch_shapes=[
            pltpu.VMEM((tiles * bs, P_CHUNK * occ), jnp.bfloat16),
            pltpu.VMEM((tiles * bs, slab), jnp.float32),
        ],
        compiler_params=pltpu.CompilerParams(vmem_limit_bytes=48 * 1024 * 1024),
        cost_estimate=pl.CostEstimate(flops=flops, transcendentals=0, bytes_accessed=bytes_accessed),
    )(tile_data, panels, slab_t)


def local(three_center, slab_factor, coefficients, tile_owner, tile_block, tile_lam):
    tile_data = three_center[0]
    n_blk = lax.axis_size("blk")
    n_aux = lax.axis_size("aux")
    tiles = tile_data.shape[0]
    per_group = tiles // n_blk
    bs = tile_data.shape[2]
    rows_dev, occ = coefficients.shape
    blocks_dev = rows_dev // bs

    owner_ids = tile_owner[0, :, 0]
    block_ids = tile_block[0]
    lam_ids = tile_lam[0]

    same_owner = owner_ids[:, None] == owner_ids[None, :]
    earlier = jnp.arange(tiles)[None, :] < jnp.arange(tiles)[:, None]
    slot_rank = jnp.sum((same_owner & earlier).astype(jnp.int32), axis=1)
    position = owner_ids * CAP + slot_rank
    slot_hit = jnp.arange(n_blk * CAP, dtype=jnp.int32)[:, None] == position[None, :]
    slot_valid = jnp.any(slot_hit, axis=1)
    slot_tile = jnp.sum(jnp.where(slot_hit, jnp.arange(tiles, dtype=jnp.int32)[None, :], 0), axis=1)

    lam_req = lax.all_to_all(lam_ids.reshape(n_blk, per_group), "blk", 0, 0, tiled=True)

    coef_blocks = coefficients.reshape(blocks_dev, bs, occ)
    send_panels = coef_blocks[lam_req.reshape(-1)].reshape(n_blk, per_group, bs, occ)
    panels = lax.all_to_all(send_panels, "blk", 0, 0, tiled=True).reshape(tiles, bs, occ)

    n_p, slab = slab_factor.shape[0], slab_factor.shape[1]
    slab_t = jnp.swapaxes(slab_factor, 1, 2).reshape(n_p * occ, slab)
    partial = tile_partials(tile_data, panels, slab_t, n_aux)
    reduced = jnp.sum(lax.all_to_all(partial, "aux", 0, 0, tiled=True), axis=0)

    me = lax.axis_index("blk")
    lists = lax.all_gather(jnp.stack([owner_ids, block_ids]), "blk", axis=0, tiled=False)
    all_owner, all_block = lists[:, 0], lists[:, 1]
    all_earlier = jnp.arange(tiles)[None, None, :] < jnp.arange(tiles)[None, :, None]
    all_rank = jnp.sum(((all_owner[:, :, None] == all_owner[:, None, :]) & all_earlier).astype(jnp.int32), axis=2)
    mine = (all_owner == me)[:, None, :] & (all_rank[:, None, :] == jnp.arange(CAP)[None, :, None])
    labels = (jnp.sum(jnp.where(mine, all_block[:, None, :] + 1, 0), axis=2) - 1).reshape(-1)

    picked = reduced[slot_tile]
    send_tiles = jnp.where(slot_valid[:, None, None], picked, 0.0)
    send_tiles = send_tiles.reshape((n_blk, CAP) + send_tiles.shape[1:])
    received = lax.all_to_all(send_tiles, "blk", 0, 0, tiled=True)
    received = received.reshape((n_blk * CAP,) + received.shape[2:])
    owned = jnp.stack(
        [jnp.sum(jnp.where((labels == b)[:, None, None], received, 0.0), axis=0) for b in range(blocks_dev)]
    )
    return owned


def solution(mesh):
    placed = (
        P("blk", None, "aux", None, None),
        P("aux", None, None),
        P("blk", None),
        P("blk", None, None),
        P("blk", None),
        P("blk", None),
    )
    return jax.shard_map(
        local, mesh=mesh, in_specs=placed, out_specs=P("blk", "aux", None), check_vma=False
    )
```

```python
import functools

import jax
import jax.numpy as jnp
from jax import lax
from jax.experimental import pallas as pl
from jax.experimental.pallas import tpu as pltpu
from jax.sharding import PartitionSpec as P

CAP = 2
P_CHUNK = 4
ROW_CHUNK = 512


def tile_kernel(t_ref, c_ref, s_ref, o_ref, hbuf, acc):
    step = pl.program_id(0)
    tiles, n_p, bs, _ = t_ref.shape
    occ = c_ref.shape[2]

    @pl.when(step == 0)
    def _():
        acc[...] = jnp.zeros_like(acc)

    for t in range(tiles):
        block = t_ref[t].reshape(n_p * bs, bs)
        half = jnp.dot(block, c_ref[t], preferred_element_type=jnp.float32).astype(jnp.bfloat16)
        for j in range(n_p):
            hbuf[t * bs:(t + 1) * bs, j * occ:(j + 1) * occ] = half[j * bs:(j + 1) * bs]
    for r in range(0, tiles * bs, ROW_CHUNK):
        acc[r:r + ROW_CHUNK] += jnp.dot(
            hbuf[r:r + ROW_CHUNK], s_ref[...], preferred_element_type=jnp.float32
        )

    @pl.when(step == pl.num_programs(0) - 1)
    def _():
        for t in range(tiles):
            o_ref[:, t] = acc[t * bs:(t + 1) * bs].T.reshape(o_ref.shape[0], o_ref.shape[2], o_ref.shape[3])


def tile_partials(tile_data, panels, slab_t, n_aux):
    tiles, n_p, bs, _ = tile_data.shape
    occ = panels.shape[2]
    slab = slab_t.shape[1]
    rows = slab // n_aux
    flops = tiles * (2 * n_p * bs * bs * occ + 2 * n_p * slab * occ * bs)
    bytes_accessed = tile_data.size * 2 + panels.size * 2 + slab_t.size * 2 + tiles * slab * bs * 4
    return pl.pallas_call(
        tile_kernel,
        grid=(n_p // P_CHUNK,),
        in_specs=[
            pl.BlockSpec((tiles, P_CHUNK, bs, bs), lambda c: (0, c, 0, 0)),
            pl.BlockSpec((tiles, bs, occ), lambda c: (0, 0, 0)),
            pl.BlockSpec((P_CHUNK * occ, slab), lambda c: (c, 0)),
        ],
        out_specs=pl.BlockSpec((n_aux, tiles, rows, bs), lambda c: (0, 0, 0, 0)),
        out_shape=jax.ShapeDtypeStruct((n_aux, tiles, rows, bs), jnp.float32),
        scratch_shapes=[
            pltpu.VMEM((tiles * bs, P_CHUNK * occ), jnp.bfloat16),
            pltpu.VMEM((tiles * bs, slab), jnp.float32),
        ],
        compiler_params=pltpu.CompilerParams(vmem_limit_bytes=48 * 1024 * 1024),
        cost_estimate=pl.CostEstimate(flops=flops, transcendentals=0, bytes_accessed=bytes_accessed),
    )(tile_data, panels, slab_t)


def local(three_center, slab_factor, coefficients, tile_owner, tile_block, tile_lam):
    tile_data = three_center[0]
    n_blk = lax.axis_size("blk")
    n_aux = lax.axis_size("aux")
    tiles = tile_data.shape[0]
    per_group = tiles // n_blk
    bs = tile_data.shape[2]
    rows_dev, occ = coefficients.shape
    blocks_dev = rows_dev // bs

    owner_ids = tile_owner[0, :, 0]
    block_ids = tile_block[0]
    lam_ids = tile_lam[0]

    lists = jnp.broadcast_to(jnp.concatenate([owner_ids, block_ids])[None, :], (n_blk, 2 * tiles))
    ints = jnp.concatenate([lam_ids.reshape(n_blk, per_group), lists], axis=1).astype(jnp.int32)
    ints_got = lax.all_to_all(ints, "blk", 0, 0, tiled=True)
    lam_req = ints_got[:, :per_group]
    all_owner = ints_got[:, per_group:per_group + tiles]
    all_block = ints_got[:, per_group + tiles:]

    coef_blocks = coefficients.reshape(blocks_dev, bs, occ)
    send_panels = coef_blocks[lam_req.reshape(-1)].reshape(n_blk, per_group, bs, occ)
    panels = lax.all_to_all(send_panels, "blk", 0, 0, tiled=True).reshape(tiles, bs, occ)

    n_p, slab = slab_factor.shape[0], slab_factor.shape[1]
    slab_t = jnp.swapaxes(slab_factor, 1, 2).reshape(n_p * occ, slab)
    partial = tile_partials(tile_data, panels, slab_t, n_aux)
    reduced = jnp.sum(lax.all_to_all(partial, "aux", 0, 0, tiled=True), axis=0)

    same_owner = owner_ids[:, None] == owner_ids[None, :]
    earlier = jnp.arange(tiles)[None, :] < jnp.arange(tiles)[:, None]
    slot_rank = jnp.sum((same_owner & earlier).astype(jnp.int32), axis=1)
    position = owner_ids * CAP + slot_rank
    slot_hit = jnp.arange(n_blk * CAP, dtype=jnp.int32)[:, None] == position[None, :]
    slot_valid = jnp.any(slot_hit, axis=1)
    slot_tile = jnp.sum(jnp.where(slot_hit, jnp.arange(tiles, dtype=jnp.int32)[None, :], 0), axis=1)

    me = lax.axis_index("blk")
    all_rank = jnp.sum(((all_owner[:, :, None] == all_owner[:, None, :]) & earlier[None]).astype(jnp.int32), axis=2)
    mine = (all_owner == me)[:, None, :] & (all_rank[:, None, :] == jnp.arange(CAP)[None, :, None])
    labels = (jnp.sum(jnp.where(mine, all_block[:, None, :] + 1, 0), axis=2) - 1).reshape(-1)

    picked = reduced[slot_tile]
    send_tiles = jnp.where(slot_valid[:, None, None], picked, 0.0)
    send_tiles = send_tiles.reshape((n_blk, CAP) + send_tiles.shape[1:])
    received = lax.all_to_all(send_tiles, "blk", 0, 0, tiled=True)
    received = received.reshape((n_blk * CAP,) + received.shape[2:])
    owned = jnp.stack(
        [jnp.sum(jnp.where((labels == b)[:, None, None], received, 0.0), axis=0) for b in range(blocks_dev)]
    )
    return owned


def solution(mesh):
    placed = (
        P("blk", None, "aux", None, None),
        P("aux", None, None),
        P("blk", None),
        P("blk", None, None),
        P("blk", None),
        P("blk", None),
    )
    return jax.shard_map(
        local, mesh=mesh, in_specs=placed, out_specs=P("blk", "aux", None), check_vma=False
    )
```

```python
import functools

import jax
import jax.numpy as jnp
from jax import lax
from jax.experimental import pallas as pl
from jax.experimental.pallas import tpu as pltpu
from jax.sharding import PartitionSpec as P

CAP = 2
P_CHUNK = 4
ROW_CHUNK = 512


def tile_kernel(t_ref, c_ref, s_ref, o_ref, hbuf, acc):
    step = pl.program_id(0)
    tiles, n_p, bs, _ = t_ref.shape
    occ = c_ref.shape[2]

    for t in range(tiles):
        block = t_ref[t].reshape(n_p * bs, bs)
        half = jnp.dot(block, c_ref[t], preferred_element_type=jnp.float32).astype(jnp.bfloat16)
        for j in range(n_p):
            hbuf[t * bs:(t + 1) * bs, j * occ:(j + 1) * occ] = half[j * bs:(j + 1) * bs]
    for r in range(0, tiles * bs, ROW_CHUNK):
        term = jnp.dot(hbuf[r:r + ROW_CHUNK], s_ref[...], preferred_element_type=jnp.float32)

        @pl.when(step == 0)
        def _():
            acc[r:r + ROW_CHUNK] = term

        @pl.when(step > 0)
        def _():
            acc[r:r + ROW_CHUNK] += term

    @pl.when(step == pl.num_programs(0) - 1)
    def _():
        for t in range(tiles):
            o_ref[:, t] = acc[t * bs:(t + 1) * bs].T.reshape(o_ref.shape[0], o_ref.shape[2], o_ref.shape[3])


def tile_partials(tile_data, panels, slab_t, n_aux):
    tiles, n_p, bs, _ = tile_data.shape
    occ = panels.shape[2]
    slab = slab_t.shape[1]
    rows = slab // n_aux
    flops = tiles * (2 * n_p * bs * bs * occ + 2 * n_p * slab * occ * bs)
    bytes_accessed = tile_data.size * 2 + panels.size * 2 + slab_t.size * 2 + tiles * slab * bs * 4
    return pl.pallas_call(
        tile_kernel,
        grid=(n_p // P_CHUNK,),
        in_specs=[
            pl.BlockSpec((tiles, P_CHUNK, bs, bs), lambda c: (0, c, 0, 0)),
            pl.BlockSpec((tiles, bs, occ), lambda c: (0, 0, 0)),
            pl.BlockSpec((P_CHUNK * occ, slab), lambda c: (c, 0)),
        ],
        out_specs=pl.BlockSpec((n_aux, tiles, rows, bs), lambda c: (0, 0, 0, 0)),
        out_shape=jax.ShapeDtypeStruct((n_aux, tiles, rows, bs), jnp.float32),
        scratch_shapes=[
            pltpu.VMEM((tiles * bs, P_CHUNK * occ), jnp.bfloat16),
            pltpu.VMEM((tiles * bs, slab), jnp.float32),
        ],
        compiler_params=pltpu.CompilerParams(vmem_limit_bytes=48 * 1024 * 1024),
        cost_estimate=pl.CostEstimate(flops=flops, transcendentals=0, bytes_accessed=bytes_accessed),
    )(tile_data, panels, slab_t)


def local(three_center, slab_factor, coefficients, tile_owner, tile_block, tile_lam):
    tile_data = three_center[0]
    n_blk = lax.axis_size("blk")
    n_aux = lax.axis_size("aux")
    tiles = tile_data.shape[0]
    per_group = tiles // n_blk
    bs = tile_data.shape[2]
    rows_dev, occ = coefficients.shape
    blocks_dev = rows_dev // bs

    owner_ids = tile_owner[0, :, 0]
    block_ids = tile_block[0]
    lam_ids = tile_lam[0]

    col = lax.broadcasted_iota(jnp.int32, (n_blk, per_group + 2 * tiles), 1)
    lists = jnp.concatenate([jnp.zeros((per_group,), jnp.int32), owner_ids, block_ids])
    if per_group == 1:
        lam_cols = jnp.broadcast_to(lam_ids[:, None], col.shape)
    else:
        lam_cols = jnp.pad(lam_ids.reshape(n_blk, per_group), ((0, 0), (0, 2 * tiles)))
    ints = jnp.where(col < per_group, lam_cols, lists[None, :]).astype(jnp.int32)
    ints_got = lax.all_to_all(ints, "blk", 0, 0, tiled=True)
    lam_req = ints_got[:, :per_group]
    all_owner = ints_got[:, per_group:per_group + tiles]
    all_block = ints_got[:, per_group + tiles:]

    coef_blocks = coefficients.reshape(blocks_dev, bs, occ)
    send_panels = coef_blocks[lam_req.reshape(-1)].reshape(n_blk, per_group, bs, occ)
    panels = lax.all_to_all(send_panels, "blk", 0, 0, tiled=True).reshape(tiles, bs, occ)

    n_p, slab = slab_factor.shape[0], slab_factor.shape[1]
    slab_t = jnp.swapaxes(slab_factor, 1, 2).reshape(n_p * occ, slab)
    partial = tile_partials(tile_data, panels, slab_t, n_aux)
    reduced = jnp.sum(lax.all_to_all(partial, "aux", 0, 0, tiled=True), axis=0)

    same_owner = owner_ids[:, None] == owner_ids[None, :]
    earlier = jnp.arange(tiles)[None, :] < jnp.arange(tiles)[:, None]
    slot_rank = jnp.sum((same_owner & earlier).astype(jnp.int32), axis=1)
    position = owner_ids * CAP + slot_rank
    slot_hit = jnp.arange(n_blk * CAP, dtype=jnp.int32)[:, None] == position[None, :]
    slot_valid = jnp.any(slot_hit, axis=1)
    slot_tile = jnp.sum(jnp.where(slot_hit, jnp.arange(tiles, dtype=jnp.int32)[None, :], 0), axis=1)

    me = lax.axis_index("blk")
    all_rank = jnp.sum(((all_owner[:, :, None] == all_owner[:, None, :]) & earlier[None]).astype(jnp.int32), axis=2)
    mine = (all_owner == me)[:, None, :] & (all_rank[:, None, :] == jnp.arange(CAP)[None, :, None])
    labels = (jnp.sum(jnp.where(mine, all_block[:, None, :] + 1, 0), axis=2) - 1).reshape(-1)

    picked = reduced[slot_tile]
    send_tiles = jnp.where(slot_valid[:, None, None], picked, 0.0)
    send_tiles = send_tiles.reshape((n_blk, CAP) + send_tiles.shape[1:])
    received = lax.all_to_all(send_tiles, "blk", 0, 0, tiled=True)
    received = received.reshape((n_blk * CAP,) + received.shape[2:])
    owned = jnp.stack(
        [jnp.sum(jnp.where((labels == b)[:, None, None], received, 0.0), axis=0) for b in range(blocks_dev)]
    )
    return owned


def solution(mesh):
    placed = (
        P("blk", None, "aux", None, None),
        P("aux", None, None),
        P("blk", None),
        P("blk", None, None),
        P("blk", None),
        P("blk", None),
    )
    return jax.shard_map(
        local, mesh=mesh, in_specs=placed, out_specs=P("blk", "aux", None), check_vma=False
    )
```

```python
import functools

import jax
import jax.numpy as jnp
from jax import lax
from jax.experimental import pallas as pl
from jax.experimental.pallas import tpu as pltpu
from jax.sharding import PartitionSpec as P

CAP = 2
P_CHUNK = 4
ROW_CHUNK = 512


def tile_kernel(t_ref, c_ref, s_ref, o_ref, hbuf, acc):
    step = pl.program_id(0)
    tiles, n_p, bs, _ = t_ref.shape
    occ = c_ref.shape[2]

    @pl.when(step == 0)
    def _():
        acc[...] = jnp.zeros_like(acc)

    for t in range(tiles):
        block = t_ref[t].reshape(n_p * bs, bs)
        half = jnp.dot(block, c_ref[t], preferred_element_type=jnp.float32).astype(jnp.bfloat16)
        for j in range(n_p):
            hbuf[t * bs:(t + 1) * bs, j * occ:(j + 1) * occ] = half[j * bs:(j + 1) * bs]
    for r in range(0, tiles * bs, ROW_CHUNK):
        acc[r:r + ROW_CHUNK] += jnp.dot(
            hbuf[r:r + ROW_CHUNK], s_ref[...], preferred_element_type=jnp.float32
        )

    @pl.when(step == pl.num_programs(0) - 1)
    def _():
        for t in range(tiles):
            o_ref[:, t] = acc[t * bs:(t + 1) * bs].T.reshape(o_ref.shape[0], o_ref.shape[2], o_ref.shape[3])


def tile_partials(tile_data, panels, slab_t, n_aux):
    tiles, n_p, bs, _ = tile_data.shape
    occ = panels.shape[2]
    slab = slab_t.shape[1]
    rows = slab // n_aux
    flops = tiles * (2 * n_p * bs * bs * occ + 2 * n_p * slab * occ * bs)
    bytes_accessed = tile_data.size * 2 + panels.size * 2 + slab_t.size * 2 + tiles * slab * bs * 4
    return pl.pallas_call(
        tile_kernel,
        grid=(n_p // P_CHUNK,),
        in_specs=[
            pl.BlockSpec((tiles, P_CHUNK, bs, bs), lambda c: (0, c, 0, 0)),
            pl.BlockSpec((tiles, bs, occ), lambda c: (0, 0, 0)),
            pl.BlockSpec((P_CHUNK * occ, slab), lambda c: (c, 0)),
        ],
        out_specs=pl.BlockSpec((n_aux, tiles, rows, bs), lambda c: (0, 0, 0, 0)),
        out_shape=jax.ShapeDtypeStruct((n_aux, tiles, rows, bs), jnp.float32),
        scratch_shapes=[
            pltpu.VMEM((tiles * bs, P_CHUNK * occ), jnp.bfloat16),
            pltpu.VMEM((tiles * bs, slab), jnp.float32),
        ],
        compiler_params=pltpu.CompilerParams(vmem_limit_bytes=48 * 1024 * 1024),
        cost_estimate=pl.CostEstimate(flops=flops, transcendentals=0, bytes_accessed=bytes_accessed),
    )(tile_data, panels, slab_t)


def local(three_center, slab_factor, coefficients, tile_owner, tile_block, tile_lam):
    tile_data = three_center[0]
    n_blk = lax.axis_size("blk")
    n_aux = lax.axis_size("aux")
    tiles = tile_data.shape[0]
    per_group = tiles // n_blk
    bs = tile_data.shape[2]
    rows_dev, occ = coefficients.shape
    blocks_dev = rows_dev // bs

    owner_ids = tile_owner[0, :, 0]
    block_ids = tile_block[0]
    lam_ids = tile_lam[0]

    lists = jnp.broadcast_to(jnp.concatenate([owner_ids, block_ids])[None, :], (n_blk, 2 * tiles))
    ints = jnp.concatenate([lam_ids.reshape(n_blk, per_group), lists], axis=1).astype(jnp.int32)
    ints_got = lax.all_to_all(ints, "blk", 0, 0, tiled=True)
    lam_req = ints_got[:, :per_group]
    all_owner = ints_got[:, per_group:per_group + tiles]
    all_block = ints_got[:, per_group + tiles:]

    coef_blocks = coefficients.reshape(blocks_dev, bs, occ)
    send_panels = coef_blocks[lam_req.reshape(-1)].reshape(n_blk, per_group, bs, occ)
    panels = lax.all_to_all(send_panels, "blk", 0, 0, tiled=True).reshape(tiles, bs, occ)

    n_p, slab = slab_factor.shape[0], slab_factor.shape[1]
    slab_t = jnp.swapaxes(slab_factor, 1, 2).reshape(n_p * occ, slab)
    half_tiles = tiles // 2
    reduced = []
    for lo in (0, half_tiles):
        part = tile_partials(tile_data[lo:lo + half_tiles], panels[lo:lo + half_tiles], slab_t, n_aux)
        reduced.append(jnp.sum(lax.all_to_all(part, "aux", 0, 0, tiled=True), axis=0))
    reduced = jnp.concatenate(reduced, axis=0)

    same_owner = owner_ids[:, None] == owner_ids[None, :]
    earlier = jnp.arange(tiles)[None, :] < jnp.arange(tiles)[:, None]
    slot_rank = jnp.sum((same_owner & earlier).astype(jnp.int32), axis=1)
    position = owner_ids * CAP + slot_rank
    slot_hit = jnp.arange(n_blk * CAP, dtype=jnp.int32)[:, None] == position[None, :]
    slot_valid = jnp.any(slot_hit, axis=1)
    slot_tile = jnp.sum(jnp.where(slot_hit, jnp.arange(tiles, dtype=jnp.int32)[None, :], 0), axis=1)

    me = lax.axis_index("blk")
    all_rank = jnp.sum(((all_owner[:, :, None] == all_owner[:, None, :]) & earlier[None]).astype(jnp.int32), axis=2)
    mine = (all_owner == me)[:, None, :] & (all_rank[:, None, :] == jnp.arange(CAP)[None, :, None])
    labels = (jnp.sum(jnp.where(mine, all_block[:, None, :] + 1, 0), axis=2) - 1).reshape(-1)

    picked = reduced[slot_tile]
    send_tiles = jnp.where(slot_valid[:, None, None], picked, 0.0)
    send_tiles = send_tiles.reshape((n_blk, CAP) + send_tiles.shape[1:])
    received = lax.all_to_all(send_tiles, "blk", 0, 0, tiled=True)
    received = received.reshape((n_blk * CAP,) + received.shape[2:])
    owned = jnp.stack(
        [jnp.sum(jnp.where((labels == b)[:, None, None], received, 0.0), axis=0) for b in range(blocks_dev)]
    )
    return owned


def solution(mesh):
    placed = (
        P("blk", None, "aux", None, None),
        P("aux", None, None),
        P("blk", None),
        P("blk", None, None),
        P("blk", None),
        P("blk", None),
    )
    return jax.shard_map(
        local, mesh=mesh, in_specs=placed, out_specs=P("blk", "aux", None), check_vma=False
    )
```

```python
import functools

import jax
import jax.numpy as jnp
from jax import lax
from jax.experimental import pallas as pl
from jax.experimental.pallas import tpu as pltpu
from jax.sharding import PartitionSpec as P

CAP = 2
P_CHUNK = 4
ROW_CHUNK = 512


def tile_kernel(t_ref, c_ref, s_ref, o_ref, hbuf, acc):
    step = pl.program_id(0)
    tiles, n_p, bs, _ = t_ref.shape
    occ = c_ref.shape[2]

    @pl.when(step == 0)
    def _():
        acc[...] = jnp.zeros_like(acc)

    for t in range(tiles):
        block = t_ref[t].reshape(n_p * bs, bs)
        half = jnp.dot(block, c_ref[t], preferred_element_type=jnp.float32).astype(jnp.bfloat16)
        for j in range(n_p):
            hbuf[t * bs:(t + 1) * bs, j * occ:(j + 1) * occ] = half[j * bs:(j + 1) * bs]
    for r in range(0, tiles * bs, ROW_CHUNK):
        acc[r:r + ROW_CHUNK] += jnp.dot(
            hbuf[r:r + ROW_CHUNK], s_ref[...], preferred_element_type=jnp.float32
        )

    @pl.when(step == pl.num_programs(0) - 1)
    def _():
        for t in range(tiles):
            o_ref[:, t] = acc[t * bs:(t + 1) * bs].T.reshape(o_ref.shape[0], o_ref.shape[2], o_ref.shape[3])


def tile_partials(tile_data, panels, slab_t, n_aux):
    tiles, n_p, bs, _ = tile_data.shape
    occ = panels.shape[2]
    slab = slab_t.shape[1]
    rows = slab // n_aux
    flops = tiles * (2 * n_p * bs * bs * occ + 2 * n_p * slab * occ * bs)
    bytes_accessed = tile_data.size * 2 + panels.size * 2 + slab_t.size * 2 + tiles * slab * bs * 4
    return pl.pallas_call(
        tile_kernel,
        grid=(n_p // P_CHUNK,),
        in_specs=[
            pl.BlockSpec((tiles, P_CHUNK, bs, bs), lambda c: (0, c, 0, 0)),
            pl.BlockSpec((tiles, bs, occ), lambda c: (0, 0, 0)),
            pl.BlockSpec((P_CHUNK * occ, slab), lambda c: (c, 0)),
        ],
        out_specs=pl.BlockSpec((n_aux, tiles, rows, bs), lambda c: (0, 0, 0, 0)),
        out_shape=jax.ShapeDtypeStruct((n_aux, tiles, rows, bs), jnp.float32),
        scratch_shapes=[
            pltpu.VMEM((tiles * bs, P_CHUNK * occ), jnp.bfloat16),
            pltpu.VMEM((tiles * bs, slab), jnp.float32),
        ],
        compiler_params=pltpu.CompilerParams(vmem_limit_bytes=48 * 1024 * 1024),
        cost_estimate=pl.CostEstimate(flops=flops, transcendentals=0, bytes_accessed=bytes_accessed),
    )(tile_data, panels, slab_t)


def local(three_center, slab_factor, coefficients, tile_owner, tile_block, tile_lam):
    tile_data = three_center[0]
    n_blk = lax.axis_size("blk")
    n_aux = lax.axis_size("aux")
    tiles = tile_data.shape[0]
    per_group = tiles // n_blk
    bs = tile_data.shape[2]
    rows_dev, occ = coefficients.shape
    blocks_dev = rows_dev // bs

    owner_ids = tile_owner[0, :, 0]
    block_ids = tile_block[0]
    lam_ids = tile_lam[0]

    lists = jnp.broadcast_to(jnp.concatenate([owner_ids, block_ids])[None, :], (n_blk, 2 * tiles))
    ints = jnp.concatenate([lam_ids.reshape(n_blk, per_group), lists], axis=1).astype(jnp.int32)
    ints_got = lax.all_to_all(ints, "blk", 0, 0, tiled=True)
    lam_req = ints_got[:, :per_group]
    all_owner = ints_got[:, per_group:per_group + tiles]
    all_block = ints_got[:, per_group + tiles:]

    coef_blocks = coefficients.reshape(blocks_dev, bs, occ)
    lam_sel = lam_req[:, :, None, None]
    send_panels = jnp.broadcast_to(coef_blocks[0], (n_blk, per_group, bs, occ))
    for b in range(1, blocks_dev):
        send_panels = jnp.where(lam_sel == b, coef_blocks[b][None, None], send_panels)
    panels = lax.all_to_all(send_panels, "blk", 0, 0, tiled=True).reshape(tiles, bs, occ)

    n_p, slab = slab_factor.shape[0], slab_factor.shape[1]
    slab_t = jnp.swapaxes(slab_factor, 1, 2).reshape(n_p * occ, slab)
    partial = tile_partials(tile_data, panels, slab_t, n_aux)
    reduced = jnp.sum(lax.all_to_all(partial, "aux", 0, 0, tiled=True), axis=0)

    same_owner = owner_ids[:, None] == owner_ids[None, :]
    earlier = jnp.arange(tiles)[None, :] < jnp.arange(tiles)[:, None]
    slot_rank = jnp.sum((same_owner & earlier).astype(jnp.int32), axis=1)
    position = owner_ids * CAP + slot_rank
    slot_hit = jnp.arange(n_blk * CAP, dtype=jnp.int32)[:, None] == position[None, :]
    slot_valid = jnp.any(slot_hit, axis=1)
    slot_tile = jnp.sum(jnp.where(slot_hit, jnp.arange(tiles, dtype=jnp.int32)[None, :], 0), axis=1)

    me = lax.axis_index("blk")
    all_rank = jnp.sum(((all_owner[:, :, None] == all_owner[:, None, :]) & earlier[None]).astype(jnp.int32), axis=2)
    mine = (all_owner == me)[:, None, :] & (all_rank[:, None, :] == jnp.arange(CAP)[None, :, None])
    labels = (jnp.sum(jnp.where(mine, all_block[:, None, :] + 1, 0), axis=2) - 1).reshape(-1)

    picked = reduced[slot_tile]
    send_tiles = jnp.where(slot_valid[:, None, None], picked, 0.0)
    send_tiles = send_tiles.reshape((n_blk, CAP) + send_tiles.shape[1:])
    received = lax.all_to_all(send_tiles, "blk", 0, 0, tiled=True)
    received = received.reshape((n_blk * CAP,) + received.shape[2:])
    owned = jnp.stack(
        [jnp.sum(jnp.where((labels == b)[:, None, None], received, 0.0), axis=0) for b in range(blocks_dev)]
    )
    return owned


def solution(mesh):
    placed = (
        P("blk", None, "aux", None, None),
        P("aux", None, None),
        P("blk", None),
        P("blk", None, None),
        P("blk", None),
        P("blk", None),
    )
    return jax.shard_map(
        local, mesh=mesh, in_specs=placed, out_specs=P("blk", "aux", None), check_vma=False
    )
```

```python
import functools

import jax
import jax.numpy as jnp
from jax import lax
from jax.experimental import pallas as pl
from jax.experimental.pallas import tpu as pltpu
from jax.sharding import PartitionSpec as P

CAP = 2
P_CHUNK = 4
ROW_CHUNK = 512


def tile_kernel(t_ref, c_ref, s_ref, o_ref, hbuf, acc):
    step = pl.program_id(0)
    tiles, n_p, bs, _ = t_ref.shape
    occ = c_ref.shape[2]

    @pl.when(step == 0)
    def _():
        acc[...] = jnp.zeros_like(acc)

    for t in range(tiles):
        block = t_ref[t].reshape(n_p * bs, bs)
        half = jnp.dot(block, c_ref[t], preferred_element_type=jnp.float32).astype(jnp.bfloat16)
        for j in range(n_p):
            hbuf[t * bs:(t + 1) * bs, j * occ:(j + 1) * occ] = half[j * bs:(j + 1) * bs]
    for r in range(0, tiles * bs, ROW_CHUNK):
        acc[r:r + ROW_CHUNK] += jnp.dot(
            hbuf[r:r + ROW_CHUNK], s_ref[...], preferred_element_type=jnp.float32
        )

    @pl.when(step == pl.num_programs(0) - 1)
    def _():
        for t in range(tiles):
            o_ref[:, t] = acc[t * bs:(t + 1) * bs].T.reshape(o_ref.shape[0], o_ref.shape[2], o_ref.shape[3])


def tile_partials(tile_data, panels, slab_t, n_aux):
    tiles, n_p, bs, _ = tile_data.shape
    occ = panels.shape[2]
    slab = slab_t.shape[1]
    rows = slab // n_aux
    flops = tiles * (2 * n_p * bs * bs * occ + 2 * n_p * slab * occ * bs)
    bytes_accessed = tile_data.size * 2 + panels.size * 2 + slab_t.size * 2 + tiles * slab * bs * 4
    return pl.pallas_call(
        tile_kernel,
        grid=(n_p // P_CHUNK,),
        in_specs=[
            pl.BlockSpec((tiles, P_CHUNK, bs, bs), lambda c: (0, c, 0, 0)),
            pl.BlockSpec((tiles, bs, occ), lambda c: (0, 0, 0)),
            pl.BlockSpec((P_CHUNK * occ, slab), lambda c: (c, 0)),
        ],
        out_specs=pl.BlockSpec((n_aux, tiles, rows, bs), lambda c: (0, 0, 0, 0)),
        out_shape=jax.ShapeDtypeStruct((n_aux, tiles, rows, bs), jnp.float32),
        scratch_shapes=[
            pltpu.VMEM((tiles * bs, P_CHUNK * occ), jnp.bfloat16),
            pltpu.VMEM((tiles * bs, slab), jnp.float32),
        ],
        compiler_params=pltpu.CompilerParams(vmem_limit_bytes=48 * 1024 * 1024),
        cost_estimate=pl.CostEstimate(flops=flops, transcendentals=0, bytes_accessed=bytes_accessed),
    )(tile_data, panels, slab_t)


def local(three_center, slab_factor, coefficients, tile_owner, tile_block, tile_lam):
    tile_data = three_center[0]
    n_blk = lax.axis_size("blk")
    n_aux = lax.axis_size("aux")
    tiles = tile_data.shape[0]
    per_group = tiles // n_blk
    bs = tile_data.shape[2]
    rows_dev, occ = coefficients.shape
    blocks_dev = rows_dev // bs

    owner_ids = tile_owner[0, :, 0]
    block_ids = tile_block[0]
    lam_ids = tile_lam[0]

    lists = jnp.broadcast_to(jnp.concatenate([owner_ids, block_ids])[None, :], (n_blk, 2 * tiles))
    ints = jnp.concatenate([lam_ids.reshape(n_blk, per_group), lists], axis=1).astype(jnp.int32)
    ints_got = lax.all_to_all(ints, "blk", 0, 0, tiled=True)
    lam_req = ints_got[:, :per_group]
    all_owner = ints_got[:, per_group:per_group + tiles]
    all_block = ints_got[:, per_group + tiles:]

    coef_blocks = coefficients.reshape(blocks_dev, bs, occ)
    send_panels = coef_blocks[lam_req.reshape(-1)].reshape(n_blk, per_group, bs, occ)
    panels = lax.all_to_all(send_panels, "blk", 0, 0, tiled=True).reshape(tiles, bs, occ)

    n_p, slab = slab_factor.shape[0], slab_factor.shape[1]
    slab_t = jnp.swapaxes(slab_factor, 1, 2).reshape(n_p * occ, slab)
    partial = tile_partials(tile_data, panels, slab_t, n_aux)
    reduced = jnp.sum(lax.all_to_all(partial, "aux", 0, 0, tiled=True), axis=0)

    same_owner = owner_ids[:, None] == owner_ids[None, :]
    earlier = jnp.arange(tiles)[None, :] < jnp.arange(tiles)[:, None]
    slot_rank = jnp.sum((same_owner & earlier).astype(jnp.int32), axis=1)
    position = owner_ids * CAP + slot_rank
    slot_hit = jnp.arange(n_blk * CAP, dtype=jnp.int32)[:, None] == position[None, :]
    slot_valid = jnp.any(slot_hit, axis=1)
    slot_tile = jnp.sum(jnp.where(slot_hit, jnp.arange(tiles, dtype=jnp.int32)[None, :], 0), axis=1)

    me = lax.axis_index("blk")
    all_rank = jnp.sum(((all_owner[:, :, None] == all_owner[:, None, :]) & earlier[None]).astype(jnp.int32), axis=2)
    mine = (all_owner == me)[:, None, :] & (all_rank[:, None, :] == jnp.arange(CAP)[None, :, None])
    labels = (jnp.sum(jnp.where(mine, all_block[:, None, :] + 1, 0), axis=2) - 1).reshape(-1)

    with_zero = jnp.concatenate([reduced, jnp.zeros((1,) + reduced.shape[1:], reduced.dtype)], axis=0)
    send_tiles = with_zero[jnp.where(slot_valid, slot_tile, tiles)]
    send_tiles = send_tiles.reshape((n_blk, CAP) + send_tiles.shape[1:])
    received = lax.all_to_all(send_tiles, "blk", 0, 0, tiled=True)
    received = received.reshape((n_blk * CAP,) + received.shape[2:])
    owned = jnp.stack(
        [jnp.sum(jnp.where((labels == b)[:, None, None], received, 0.0), axis=0) for b in range(blocks_dev)]
    )
    return owned


def solution(mesh):
    placed = (
        P("blk", None, "aux", None, None),
        P("aux", None, None),
        P("blk", None),
        P("blk", None, None),
        P("blk", None),
        P("blk", None),
    )
    return jax.shard_map(
        local, mesh=mesh, in_specs=placed, out_specs=P("blk", "aux", None), check_vma=False
    )
```

```python
import functools

import jax
import jax.numpy as jnp
from jax import lax
from jax.experimental import pallas as pl
from jax.experimental.pallas import tpu as pltpu
from jax.sharding import PartitionSpec as P

CAP = 2
P_CHUNK = 8
ROW_CHUNK = 512


def tile_kernel(t_ref, c_ref, s_ref, o_ref, hbuf, acc):
    step = pl.program_id(0)
    tiles, n_p, bs, _ = t_ref.shape
    occ = c_ref.shape[2]

    @pl.when(step == 0)
    def _():
        acc[...] = jnp.zeros_like(acc)

    for t in range(tiles):
        block = t_ref[t].reshape(n_p * bs, bs)
        half = jnp.dot(block, c_ref[t], preferred_element_type=jnp.float32).astype(jnp.bfloat16)
        for j in range(n_p):
            hbuf[t * bs:(t + 1) * bs, j * occ:(j + 1) * occ] = half[j * bs:(j + 1) * bs]
    for r in range(0, tiles * bs, ROW_CHUNK):
        acc[r:r + ROW_CHUNK] += jnp.dot(
            hbuf[r:r + ROW_CHUNK], s_ref[...], preferred_element_type=jnp.float32
        )

    @pl.when(step == pl.num_programs(0) - 1)
    def _():
        for t in range(tiles):
            o_ref[:, t] = acc[t * bs:(t + 1) * bs].T.reshape(o_ref.shape[0], o_ref.shape[2], o_ref.shape[3])


def tile_partials(tile_data, panels, slab_t, n_aux):
    tiles, n_p, bs, _ = tile_data.shape
    occ = panels.shape[2]
    slab = slab_t.shape[1]
    rows = slab // n_aux
    flops = tiles * (2 * n_p * bs * bs * occ + 2 * n_p * slab * occ * bs)
    bytes_accessed = tile_data.size * 2 + panels.size * 2 + slab_t.size * 2 + tiles * slab * bs * 4
    return pl.pallas_call(
        tile_kernel,
        grid=(n_p // P_CHUNK,),
        in_specs=[
            pl.BlockSpec((tiles, P_CHUNK, bs, bs), lambda c: (0, c, 0, 0)),
            pl.BlockSpec((tiles, bs, occ), lambda c: (0, 0, 0)),
            pl.BlockSpec((P_CHUNK * occ, slab), lambda c: (c, 0)),
        ],
        out_specs=pl.BlockSpec((n_aux, tiles, rows, bs), lambda c: (0, 0, 0, 0)),
        out_shape=jax.ShapeDtypeStruct((n_aux, tiles, rows, bs), jnp.float32),
        scratch_shapes=[
            pltpu.VMEM((tiles * bs, P_CHUNK * occ), jnp.bfloat16),
            pltpu.VMEM((tiles * bs, slab), jnp.float32),
        ],
        compiler_params=pltpu.CompilerParams(vmem_limit_bytes=48 * 1024 * 1024),
        cost_estimate=pl.CostEstimate(flops=flops, transcendentals=0, bytes_accessed=bytes_accessed),
    )(tile_data, panels, slab_t)


def local(three_center, slab_factor, coefficients, tile_owner, tile_block, tile_lam):
    tile_data = three_center[0]
    n_blk = lax.axis_size("blk")
    n_aux = lax.axis_size("aux")
    tiles = tile_data.shape[0]
    per_group = tiles // n_blk
    bs = tile_data.shape[2]
    rows_dev, occ = coefficients.shape
    blocks_dev = rows_dev // bs

    owner_ids = tile_owner[0, :, 0]
    block_ids = tile_block[0]
    lam_ids = tile_lam[0]

    lists = jnp.broadcast_to(jnp.concatenate([owner_ids, block_ids])[None, :], (n_blk, 2 * tiles))
    ints = jnp.concatenate([lam_ids.reshape(n_blk, per_group), lists], axis=1).astype(jnp.int32)
    ints_got = lax.all_to_all(ints, "blk", 0, 0, tiled=True)
    lam_req = ints_got[:, :per_group]
    all_owner = ints_got[:, per_group:per_group + tiles]
    all_block = ints_got[:, per_group + tiles:]

    coef_blocks = coefficients.reshape(blocks_dev, bs, occ)
    send_panels = coef_blocks[lam_req.reshape(-1)].reshape(n_blk, per_group, bs, occ)
    panels = lax.all_to_all(send_panels, "blk", 0, 0, tiled=True).reshape(tiles, bs, occ)

    n_p, slab = slab_factor.shape[0], slab_factor.shape[1]
    slab_t = jnp.swapaxes(slab_factor, 1, 2).reshape(n_p * occ, slab)
    partial = tile_partials(tile_data, panels, slab_t, n_aux)
    reduced = jnp.sum(lax.all_to_all(partial, "aux", 0, 0, tiled=True), axis=0)

    same_owner = owner_ids[:, None] == owner_ids[None, :]
    earlier = jnp.arange(tiles)[None, :] < jnp.arange(tiles)[:, None]
    slot_rank = jnp.sum((same_owner & earlier).astype(jnp.int32), axis=1)
    position = owner_ids * CAP + slot_rank
    slot_hit = jnp.arange(n_blk * CAP, dtype=jnp.int32)[:, None] == position[None, :]
    slot_valid = jnp.any(slot_hit, axis=1)
    slot_tile = jnp.sum(jnp.where(slot_hit, jnp.arange(tiles, dtype=jnp.int32)[None, :], 0), axis=1)

    me = lax.axis_index("blk")
    all_rank = jnp.sum(((all_owner[:, :, None] == all_owner[:, None, :]) & earlier[None]).astype(jnp.int32), axis=2)
    mine = (all_owner == me)[:, None, :] & (all_rank[:, None, :] == jnp.arange(CAP)[None, :, None])
    labels = (jnp.sum(jnp.where(mine, all_block[:, None, :] + 1, 0), axis=2) - 1).reshape(-1)

    picked = reduced[slot_tile]
    send_tiles = jnp.where(slot_valid[:, None, None], picked, 0.0)
    send_tiles = send_tiles.reshape((n_blk, CAP) + send_tiles.shape[1:])
    received = lax.all_to_all(send_tiles, "blk", 0, 0, tiled=True)
    received = received.reshape((n_blk * CAP,) + received.shape[2:])
    owned = jnp.stack(
        [jnp.sum(jnp.where((labels == b)[:, None, None], received, 0.0), axis=0) for b in range(blocks_dev)]
    )
    return owned


def solution(mesh):
    placed = (
        P("blk", None, "aux", None, None),
        P("aux", None, None),
        P("blk", None),
        P("blk", None, None),
        P("blk", None),
        P("blk", None),
    )
    return jax.shard_map(
        local, mesh=mesh, in_specs=placed, out_specs=P("blk", "aux", None), check_vma=False
    )
```
